256 devices in a mesh: sample: 16 (over y, x_hi, core), filter: 16 (over x_lo, z).
Axes of the slice: x: 4 (x_hi: 2, x_lo: 2; x = x_hi * 2 + x_lo), y: 4, z: 8, core: 2. Of those that a mesh axis runs over, the one named last changes fastest.
Arguments:
- activations: bfloat16 [16, 2, 128, 2048], P('sample', None, None, 'filter'), may hold values from -18 to 18
- cotangent: bfloat16 [16, 2, 128, 2048], P('sample', None, None, 'filter'), may hold values from -2.5 to 2.5
- master_first: float32 [9, 2048, 2048], P(None, 'sample', 'filter'), may hold values from -0.046875 to 0.046875
- moment_first: float32 [9, 2048, 2048], P(None, 'sample', 'filter'), may hold values from -6 to 6
- second_first: float32 [9, 2048, 2048], P(None, 'sample', 'filter'), may hold values from 0.05 to 1
- master_second: float32 [9, 2048, 2048], P(None, 'sample', 'filter'), may hold values from -0.046875 to 0.046875
- moment_second: float32 [9, 2048, 2048], P(None, 'sample', 'filter'), may hold values from -6 to 6
- second_second: float32 [9, 2048, 2048], P(None, 'sample', 'filter'), may hold values from 0.05 to 1
Outputs:
- level_out: bfloat16 [16, 2, 128, 2048], P('sample', None, None, 'filter')
- input_grad: bfloat16 [16, 2, 128, 2048], P('sample', None, None, 'filter')
- new_master_first: float32 [9, 2048, 2048], P(None, 'sample', 'filter')
- new_moment_first: float32 [9, 2048, 2048], P(None, 'sample', 'filter')
- new_second_first: float32 [9, 2048, 2048], P(None, 'sample', 'filter')
- new_master_second: float32 [9, 2048, 2048], P(None, 'sample', 'filter')
- new_moment_second: float32 [9, 2048, 2048], P(None, 'sample', 'filter')
- new_second_second: float32 [9, 2048, 2048], P(None, 'sample', 'filter')
The draws below stay inside these ranges and needn't reach their ends.
All inputs are finite; a program needn't handle non-finite values.
Results may differ from the reference program's by a relative error of at most 0.017.
Values may be sent and summed in bfloat16 or wider, within the bound.
No kernel may reach another device: no remote copies, remote signals or barrier semaphores. Data moves between devices by JAX's collectives and lax.ppermute only.
A program may use at most 128 MiB of HBM per device.

```python
import math
import jax
import jax.numpy as jnp
from jax import lax

C = 2048
GROUP = 64
ROWS = 2
COLS = 128
SAMPLES = 16
N_FILTER = 16


def draw_activations(key, part):
    key_base, key_cell = jax.random.split(key, 2)
    base_noise = jnp.clip(jax.random.normal(key_base, (SAMPLES, ROWS, COLS, C), jnp.float32), -6.0, 6.0)
    cell_scale = jnp.exp(jax.random.uniform(key_cell, (SAMPLES, ROWS, COLS, 1), jnp.float32, math.log(0.2), math.log(2.0)))
    return (base_noise * cell_scale).astype(jnp.bfloat16)


def block_levels(key, extent, shards, least, top_value):
    def one(dim, shards_of):
        draws = jax.random.uniform(jax.random.fold_in(jax.random.fold_in(key, 6), dim), (shards_of,), jnp.float32, least / len(shards), top_value / len(shards))
        return jnp.repeat(jnp.exp(draws), extent[dim] // shards_of).reshape((-1,) + (1,) * (len(extent) - dim - 1))

    factor_of = one(*shards[0])
    for cut in shards[1:]:
        factor_of = factor_of * one(*cut)
    return factor_of


def normal_values(rng, dims, scale, most, cuts=(), dtype=jnp.bfloat16):
    loudness = block_levels(rng, dims, cuts, -0.22, 0.18) if cuts else 1.0
    result = jax.random.normal(rng, dims, jnp.float32) * scale * loudness
    return jnp.minimum(jnp.maximum(result, -most), most).astype(dtype)


def setup_inputs(seed: int = 0) -> dict:
    key_list = jax.random.split(jax.random.key(seed), 9)
    activations = draw_activations(jax.random.fold_in(key_list[8], 71), 0)
    cotangent = normal_values(key_list[1], (SAMPLES, ROWS, COLS, C), 0.25, 2.5, ((0, 16), (3, 16)))
    master_first = normal_values(key_list[2], (9, C, C), (9 * C) ** -0.5, 0.046875, ((1, 16), (2, 16)), jnp.float32)
    moment_first = normal_values(key_list[3], (9, C, C), 1.0, 6.0, ((1, 16), (2, 16)), jnp.float32)
    second_first = jnp.clip(jnp.exp(math.log(1.0) - 2.9957323 * jax.random.uniform(key_list[4], (9, C, C), jnp.float32) ** block_levels(key_list[4], (9, C, C), ((1, 16), (2, 16)), -0.2, 0.2)), 0.05, 1.0)
    master_second = normal_values(key_list[5], (9, C, C), (9 * C) ** -0.5, 0.046875, ((1, 16), (2, 16)), jnp.float32)
    moment_second = normal_values(key_list[6], (9, C, C), 1.0, 6.0, ((1, 16), (2, 16)), jnp.float32)
    second_second = jnp.clip(jnp.exp(math.log(1.0) - 2.9957323 * jax.random.uniform(key_list[7], (9, C, C), jnp.float32) ** block_levels(key_list[7], (9, C, C), ((1, 16), (2, 16)), -0.2, 0.2)), 0.05, 1.0)
    return dict(activations=activations, cotangent=cotangent, master_first=master_first, moment_first=moment_first, second_first=second_first, master_second=master_second, moment_second=moment_second, second_second=second_second)


NORM_EPS = 1e-05
LEARN_RATE = 0.001
BETA_ONE = 0.9
BETA_TWO = 0.999
ADAM_EPS = 1e-08
CORRECT_ONE = 1.0 - 0.9 ** 10
CORRECT_TWO = 1.0 - 0.999 ** 10

def pad_slab(field):
    return jnp.pad(field, ((0, 0), (1, 1), (1, 1), (0, 0)))

def window(padded, row_start, column_start, height, breadth):
    return padded[:, row_start:row_start + height, column_start:column_start + breadth, :]

def conv_forward(source, weight):
    samples, height, breadth, depth_in = source.shape
    padded = pad_slab(source)
    summed = jnp.zeros((samples * height * breadth, weight.shape[2]), jnp.float32)
    for kernel_tap in range(9):
        shifted = window(padded, kernel_tap // 3, kernel_tap % 3, height, breadth)
        summed = summed + jnp.dot(shifted.reshape(samples * height * breadth, depth_in), weight[kernel_tap], preferred_element_type=jnp.float32)
    return summed.reshape(samples, height, breadth, weight.shape[2])

def rounded(values):
    return lax.optimization_barrier(values.astype(jnp.bfloat16)).astype(jnp.float32)

def adjoint_block(upstream, weight):
    samples, height, breadth, depth_out = upstream.shape
    padded = pad_slab(upstream)
    summed = jnp.zeros((samples * height * breadth, weight.shape[1]), jnp.float32)
    for kernel_tap in range(9):
        shifted = window(padded, 2 - kernel_tap // 3, 2 - kernel_tap % 3, height, breadth)
        summed = summed + lax.dot_general(shifted.reshape(samples * height * breadth, depth_out), weight[kernel_tap], (((1,), (1,)), ((), ())), preferred_element_type=jnp.float32)
    return summed.reshape(samples, height, breadth, weight.shape[1])

def conv_adjoint(upstream, weight):
    block_width = upstream.shape[3] // N_FILTER
    total = jnp.zeros(upstream.shape[:3] + (weight.shape[1],), jnp.float32)
    for block in range(N_FILTER):
        piece = upstream[:, :, :, block * block_width:(block + 1) * block_width]
        taps = weight[:, :, block * block_width:(block + 1) * block_width]
        total = total + rounded(adjoint_block(piece, taps))
    return total

def group_silu(pre_act):
    samples, height, breadth, depth_all = pre_act.shape
    grouped = pre_act.reshape(samples, height, breadth, depth_all // GROUP, GROUP)
    center = lax.optimization_barrier(jnp.mean(grouped, axis=(1, 2, 4), keepdims=True))
    deviation = grouped - center
    spread = lax.optimization_barrier(jnp.mean(deviation * deviation, axis=(1, 2, 4), keepdims=True))
    return jax.nn.silu(deviation * lax.rsqrt(spread + NORM_EPS)).reshape(pre_act.shape)

def tap_grads(source, upstream):
    samples, height, breadth, depth_in = source.shape
    padded = pad_slab(source)
    flat_up = upstream.reshape(samples, height * breadth, upstream.shape[3]).astype(jnp.float32)
    results = []
    for kernel_tap in range(9):
        shifted = window(padded, kernel_tap // 3, kernel_tap % 3, height, breadth).reshape(samples, height * breadth, depth_in)
        results.append(lax.dot_general(shifted.astype(jnp.float32), flat_up, (((1,), (1,)), ((0,), (0,))), preferred_element_type=jnp.float32))
    return jnp.stack(results, axis=1)

def sample_sum(source, upstream):

    def accumulate(running, sample_pair):
        per_sample = tap_grads(sample_pair[0][None], sample_pair[1][None])
        return (running + lax.optimization_barrier(jnp.sum(rounded(per_sample), axis=0)), None)
    start_value = jnp.zeros((9, source.shape[3], upstream.shape[3]), jnp.float32)
    summed, _ = lax.scan(accumulate, start_value, (source, upstream))
    return summed

def adam_update(master, moment, second, gradient):
    moment_new = BETA_ONE * moment + (1.0 - BETA_ONE) * gradient
    second_new = BETA_TWO * second + (1.0 - BETA_TWO) * gradient * gradient
    step_size = moment_new / CORRECT_ONE / (jnp.sqrt(second_new / CORRECT_TWO) + ADAM_EPS)
    return (master - LEARN_RATE * step_size, moment_new, second_new)

def reference(activations, cotangent, master_first, moment_first, second_first, master_second, moment_second, second_second):
    weight_first = master_first.astype(jnp.bfloat16)
    weight_second = master_second.astype(jnp.bfloat16)
    pre_first = conv_forward(activations, weight_first)
    hidden = group_silu(pre_first).astype(jnp.bfloat16)
    pre_second = conv_forward(hidden, weight_second)
    level_out = (activations.astype(jnp.float32) + pre_second).astype(jnp.bfloat16)
    hidden_grad = conv_adjoint(cotangent, weight_second)
    _, pullback = jax.vjp(group_silu, pre_first)
    pre_grad = pullback(hidden_grad)[0].astype(jnp.bfloat16)
    input_grad = (cotangent.astype(jnp.float32) + conv_adjoint(pre_grad, weight_first)).astype(jnp.bfloat16)
    grad_second = sample_sum(hidden, cotangent)
    grad_first = sample_sum(activations, pre_grad)
    new_master_first, new_moment_first, new_second_first = adam_update(master_first, moment_first, second_first, grad_first)
    new_master_second, new_moment_second, new_second_second = adam_update(master_second, moment_second, second_second, grad_second)
    return (level_out, input_grad, new_master_first, new_moment_first, new_second_first, new_master_second, new_moment_second, new_second_second)
```

```python
import jax
import jax.numpy as jnp
from jax import lax
from jax.sharding import PartitionSpec as P

GROUP = 64

NORM_EPS = 1e-05
LEARN_RATE = 0.001
BETA_ONE = 0.9
BETA_TWO = 0.999
ADAM_EPS = 1e-08
CORRECT_ONE = 1.0 - 0.9**10
CORRECT_TWO = 1.0 - 0.999**10


def pad_slab(field):
    return jnp.pad(field, ((0, 0), (1, 1), (1, 1), (0, 0)))


def window(padded, row_start, column_start, height, breadth):
    return padded[:, row_start : row_start + height, column_start : column_start + breadth, :]


def conv_forward(source, weight):
    samples, height, breadth, depth_in = source.shape
    padded = pad_slab(source)
    summed = jnp.zeros((samples * height * breadth, weight.shape[2]), jnp.float32)
    for kernel_tap in range(9):
        shifted = window(padded, kernel_tap // 3, kernel_tap % 3, height, breadth)
        summed = summed + jnp.dot(
            shifted.reshape(samples * height * breadth, depth_in),
            weight[kernel_tap],
            preferred_element_type=jnp.float32,
        )
    return summed.reshape(samples, height, breadth, weight.shape[2])


def adjoint_block(upstream, weight):
    samples, height, breadth, depth_out = upstream.shape
    padded = pad_slab(upstream)
    summed = jnp.zeros((samples * height * breadth, weight.shape[1]), jnp.float32)
    for kernel_tap in range(9):
        shifted = window(padded, 2 - kernel_tap // 3, 2 - kernel_tap % 3, height, breadth)
        summed = summed + lax.dot_general(
            shifted.reshape(samples * height * breadth, depth_out),
            weight[kernel_tap],
            (((1,), (1,)), ((), ())),
            preferred_element_type=jnp.float32,
        )
    return summed.reshape(samples, height, breadth, weight.shape[1])


def group_silu(pre_act):
    samples, height, breadth, depth_all = pre_act.shape
    grouped = pre_act.reshape(samples, height, breadth, depth_all // GROUP, GROUP)
    center = jnp.mean(grouped, axis=(1, 2, 4), keepdims=True)
    deviation = grouped - center
    spread = jnp.mean(deviation * deviation, axis=(1, 2, 4), keepdims=True)
    return jax.nn.silu(deviation * lax.rsqrt(spread + NORM_EPS)).reshape(pre_act.shape)


def tap_grad_sum(source, upstream):
    samples, height, breadth, depth_in = source.shape
    padded = pad_slab(source)
    flat_up = upstream.reshape(samples, height * breadth, upstream.shape[3])
    results = []
    for kernel_tap in range(9):
        shifted = window(padded, kernel_tap // 3, kernel_tap % 3, height, breadth).reshape(
            samples, height * breadth, depth_in
        )
        per_sample = lax.dot_general(
            shifted, flat_up, (((1,), (1,)), ((0,), (0,))), preferred_element_type=jnp.float32
        )
        results.append(jnp.sum(per_sample.astype(jnp.bfloat16).astype(jnp.float32), axis=0))
    return jnp.stack(results, axis=0)


def adam_update(master, moment, second, gradient):
    moment_new = BETA_ONE * moment + (1.0 - BETA_ONE) * gradient
    second_new = BETA_TWO * second + (1.0 - BETA_TWO) * gradient * gradient
    step_size = moment_new / CORRECT_ONE / (jnp.sqrt(second_new / CORRECT_TWO) + ADAM_EPS)
    return (master - LEARN_RATE * step_size, moment_new, second_new)


def transpose_mesh(block):
    count = lax.axis_size("sample")
    pairs = [(row * count + col, col * count + row) for row in range(count) for col in range(count)]
    return lax.ppermute(block, ("sample", "filter"), pairs)


def gather_along(block, axis):
    count = lax.axis_size(axis)
    return lax.all_to_all(jnp.tile(block, (count, 1, 1, 1)), axis, 0, 0, tiled=True)


def sum_scatter_along(blocks, axis):
    count = lax.axis_size(axis)
    pieces = lax.all_to_all(blocks, axis, 0, 0, tiled=True)
    return jnp.sum(pieces.astype(jnp.float32).reshape((count,) + blocks.shape[1:]), axis=0, keepdims=True)


def forward_conv(field, weight):
    whole = gather_along(transpose_mesh(field), "filter")
    partial = conv_forward(whole, weight)
    return whole, sum_scatter_along(partial, "sample")


def adjoint_conv(upstream_whole, weight):
    terms = adjoint_block(upstream_whole, weight).astype(jnp.bfloat16)
    return transpose_mesh(sum_scatter_along(terms, "filter"))


def per_device(
    activations,
    cotangent,
    master_first,
    moment_first,
    second_first,
    master_second,
    moment_second,
    second_second,
):
    weight_first = master_first.astype(jnp.bfloat16)
    weight_second = master_second.astype(jnp.bfloat16)
    whole_cotangent = gather_along(cotangent, "sample")
    whole_input, pre_first = forward_conv(activations, weight_first)
    hidden = group_silu(pre_first).astype(jnp.bfloat16)
    whole_hidden, pre_second = forward_conv(hidden, weight_second)
    level_out = (activations.astype(jnp.float32) + pre_second).astype(jnp.bfloat16)
    hidden_grad = adjoint_conv(whole_cotangent, weight_second)
    _, pullback = jax.vjp(group_silu, pre_first)
    pre_grad = pullback(hidden_grad)[0].astype(jnp.bfloat16)
    whole_pre_grad = gather_along(pre_grad, "sample")
    input_grad = (cotangent.astype(jnp.float32) + adjoint_conv(whole_pre_grad, weight_first)).astype(
        jnp.bfloat16
    )
    grad_second = tap_grad_sum(whole_hidden, whole_cotangent)
    grad_first = tap_grad_sum(whole_input, whole_pre_grad)
    new_master_first, new_moment_first, new_second_first = adam_update(
        master_first, moment_first, second_first, grad_first
    )
    new_master_second, new_moment_second, new_second_second = adam_update(
        master_second, moment_second, second_second, grad_second
    )
    return (
        level_out,
        input_grad,
        new_master_first,
        new_moment_first,
        new_second_first,
        new_master_second,
        new_moment_second,
        new_second_second,
    )


def solution(mesh):
    field = P("sample", None, None, "filter")
    taps = P(None, "sample", "filter")
    return jax.shard_map(
        per_device,
        mesh=mesh,
        in_specs=(field, field, taps, taps, taps, taps, taps, taps),
        out_specs=(field, field, taps, taps, taps, taps, taps, taps),
        check_vma=False,
    )
```

```python
import jax
import jax.numpy as jnp
from jax import lax
from jax.sharding import PartitionSpec as P

GROUP = 64

NORM_EPS = 1e-05
LEARN_RATE = 0.001
BETA_ONE = 0.9
BETA_TWO = 0.999
ADAM_EPS = 1e-08
CORRECT_ONE = 1.0 - 0.9**10
CORRECT_TWO = 1.0 - 0.999**10


def pad_slab(field):
    return jnp.pad(field, ((0, 0), (1, 1), (1, 1), (0, 0)))


def window(padded, row_start, column_start, height, breadth):
    return padded[:, row_start : row_start + height, column_start : column_start + breadth, :]


def conv_forward(source, weight):
    samples, height, breadth, depth_in = source.shape
    padded = pad_slab(source)
    summed = jnp.zeros((samples * height * breadth, weight.shape[2]), jnp.float32)
    for kernel_tap in range(9):
        shifted = window(padded, kernel_tap // 3, kernel_tap % 3, height, breadth)
        summed = summed + jnp.dot(
            shifted.reshape(samples * height * breadth, depth_in),
            weight[kernel_tap],
            preferred_element_type=jnp.float32,
        )
    return summed.reshape(samples, height, breadth, weight.shape[2])


def adjoint_block(upstream, weight):
    samples, height, breadth, depth_out = upstream.shape
    padded = pad_slab(upstream)
    summed = jnp.zeros((samples * height * breadth, weight.shape[1]), jnp.float32)
    for kernel_tap in range(9):
        shifted = window(padded, 2 - kernel_tap // 3, 2 - kernel_tap % 3, height, breadth)
        summed = summed + lax.dot_general(
            shifted.reshape(samples * height * breadth, depth_out),
            weight[kernel_tap],
            (((1,), (1,)), ((), ())),
            preferred_element_type=jnp.float32,
        )
    return summed.reshape(samples, height, breadth, weight.shape[1])


def group_silu(pre_act):
    samples, height, breadth, depth_all = pre_act.shape
    grouped = pre_act.reshape(samples, height, breadth, depth_all // GROUP, GROUP)
    center = jnp.mean(grouped, axis=(1, 2, 4), keepdims=True)
    deviation = grouped - center
    spread = jnp.mean(deviation * deviation, axis=(1, 2, 4), keepdims=True)
    return jax.nn.silu(deviation * lax.rsqrt(spread + NORM_EPS)).reshape(pre_act.shape)


def tap_grad_sum(source, upstream):
    samples, height, breadth, depth_in = source.shape
    padded = pad_slab(source)
    flat_up = upstream.reshape(samples, height * breadth, upstream.shape[3])
    results = []
    for kernel_tap in range(9):
        shifted = window(padded, kernel_tap // 3, kernel_tap % 3, height, breadth).reshape(
            samples, height * breadth, depth_in
        )
        per_sample = lax.dot_general(
            shifted, flat_up, (((1,), (1,)), ((0,), (0,))), preferred_element_type=jnp.float32
        )
        results.append(jnp.sum(per_sample.astype(jnp.bfloat16).astype(jnp.float32), axis=0))
    return jnp.stack(results, axis=0)


def adam_update(master, moment, second, gradient):
    moment_new = BETA_ONE * moment + (1.0 - BETA_ONE) * gradient
    second_new = BETA_TWO * second + (1.0 - BETA_TWO) * gradient * gradient
    step_size = moment_new / CORRECT_ONE / (jnp.sqrt(second_new / CORRECT_TWO) + ADAM_EPS)
    return (master - LEARN_RATE * step_size, moment_new, second_new)


def transpose_mesh(block):
    count = lax.axis_size("sample")
    pairs = [(row * count + col, col * count + row) for row in range(count) for col in range(count)]
    return lax.ppermute(block, ("sample", "filter"), pairs)


def gather_along(block, axis):
    count = lax.axis_size(axis)
    return lax.all_to_all(jnp.tile(block, (count, 1, 1, 1)), axis, 0, 0, tiled=True)


def sum_scatter_along(blocks, axis):
    count = lax.axis_size(axis)
    pieces = lax.all_to_all(blocks, axis, 0, 0, tiled=True)
    return jnp.sum(pieces.astype(jnp.float32).reshape((count,) + blocks.shape[1:]), axis=0, keepdims=True)


def gather_pairs(block, axis):
    count = lax.axis_size(axis)
    mine = lax.axis_index(axis)
    whole = block
    step = 1
    while step < count:
        other = lax.ppermute(whole, axis, [(j, j ^ step) for j in range(count)])
        upper = (mine // step) % 2 == 1
        whole = jnp.where(upper, jnp.concatenate([other, whole]), jnp.concatenate([whole, other]))
        step *= 2
    return whole


def sum_scatter_pairs(blocks, axis):
    count = lax.axis_size(axis)
    mine = lax.axis_index(axis)
    running = blocks.astype(jnp.float32)
    step = count // 2
    while step >= 1:
        upper = (mine // step) % 2
        keep = lax.dynamic_slice_in_dim(running, upper * step, step, axis=0)
        send = lax.dynamic_slice_in_dim(running, (1 - upper) * step, step, axis=0)
        running = keep + lax.ppermute(send, axis, [(j, j ^ step) for j in range(count)])
        step //= 2
    return running


def forward_conv(field, weight):
    whole = gather_along(transpose_mesh(field), "filter")
    partial = conv_forward(whole, weight)
    return whole, sum_scatter_pairs(partial, "sample")


def adjoint_conv(upstream_whole, weight):
    terms = adjoint_block(upstream_whole, weight).astype(jnp.bfloat16)
    return transpose_mesh(sum_scatter_along(terms, "filter"))


def per_device(
    activations,
    cotangent,
    master_first,
    moment_first,
    second_first,
    master_second,
    moment_second,
    second_second,
):
    weight_first = master_first.astype(jnp.bfloat16)
    weight_second = master_second.astype(jnp.bfloat16)
    whole_cotangent = gather_pairs(cotangent, "sample")
    whole_input, pre_first = forward_conv(activations, weight_first)
    hidden = group_silu(pre_first).astype(jnp.bfloat16)
    whole_hidden, pre_second = forward_conv(hidden, weight_second)
    level_out = (activations.astype(jnp.float32) + pre_second).astype(jnp.bfloat16)
    hidden_grad = adjoint_conv(whole_cotangent, weight_second)
    _, pullback = jax.vjp(group_silu, pre_first)
    pre_grad = pullback(hidden_grad)[0].astype(jnp.bfloat16)
    whole_pre_grad = gather_pairs(pre_grad, "sample")
    input_grad = (cotangent.astype(jnp.float32) + adjoint_conv(whole_pre_grad, weight_first)).astype(
        jnp.bfloat16
    )
    grad_second = tap_grad_sum(whole_hidden, whole_cotangent)
    grad_first = tap_grad_sum(whole_input, whole_pre_grad)
    new_master_first, new_moment_first, new_second_first = adam_update(
        master_first, moment_first, second_first, grad_first
    )
    new_master_second, new_moment_second, new_second_second = adam_update(
        master_second, moment_second, second_second, grad_second
    )
    return (
        level_out,
        input_grad,
        new_master_first,
        new_moment_first,
        new_second_first,
        new_master_second,
        new_moment_second,
        new_second_second,
    )


def solution(mesh):
    field = P("sample", None, None, "filter")
    taps = P(None, "sample", "filter")
    return jax.shard_map(
        per_device,
        mesh=mesh,
        in_specs=(field, field, taps, taps, taps, taps, taps, taps),
        out_specs=(field, field, taps, taps, taps, taps, taps, taps),
        check_vma=False,
    )
```

```python
import jax
import jax.numpy as jnp
from jax import lax
from jax.sharding import PartitionSpec as P

GROUP = 64

NORM_EPS = 1e-05
LEARN_RATE = 0.001
BETA_ONE = 0.9
BETA_TWO = 0.999
ADAM_EPS = 1e-08
CORRECT_ONE = 1.0 - 0.9**10
CORRECT_TWO = 1.0 - 0.999**10


def pad_slab(field):
    return jnp.pad(field, ((0, 0), (1, 1), (1, 1), (0, 0)))


def window(padded, row_start, column_start, height, breadth):
    return padded[:, row_start : row_start + height, column_start : column_start + breadth, :]


def conv_forward(source, weight):
    samples, height, breadth, depth_in = source.shape
    padded = pad_slab(source)
    summed = jnp.zeros((samples * height * breadth, weight.shape[2]), jnp.float32)
    for kernel_tap in range(9):
        shifted = window(padded, kernel_tap // 3, kernel_tap % 3, height, breadth)
        summed = summed + jnp.dot(
            shifted.reshape(samples * height * breadth, depth_in),
            weight[kernel_tap],
            preferred_element_type=jnp.float32,
        )
    return summed.reshape(samples, height, breadth, weight.shape[2])


def adjoint_block(upstream, weight):
    samples, height, breadth, depth_out = upstream.shape
    padded = pad_slab(upstream)
    summed = jnp.zeros((samples * height * breadth, weight.shape[1]), jnp.float32)
    for kernel_tap in range(9):
        shifted = window(padded, 2 - kernel_tap // 3, 2 - kernel_tap % 3, height, breadth)
        summed = summed + lax.dot_general(
            shifted.reshape(samples * height * breadth, depth_out),
            weight[kernel_tap],
            (((1,), (1,)), ((), ())),
            preferred_element_type=jnp.float32,
        )
    return summed.reshape(samples, height, breadth, weight.shape[1])


def group_silu(pre_act):
    samples, height, breadth, depth_all = pre_act.shape
    grouped = pre_act.reshape(samples, height, breadth, depth_all // GROUP, GROUP)
    center = jnp.mean(grouped, axis=(1, 2, 4), keepdims=True)
    deviation = grouped - center
    spread = jnp.mean(deviation * deviation, axis=(1, 2, 4), keepdims=True)
    return jax.nn.silu(deviation * lax.rsqrt(spread + NORM_EPS)).reshape(pre_act.shape)


def tap_grad_sum(source, upstream):
    samples, height, breadth, depth_in = source.shape
    padded = pad_slab(source)
    flat_up = upstream.reshape(samples, height * breadth, upstream.shape[3])
    results = []
    for kernel_tap in range(9):
        shifted = window(padded, kernel_tap // 3, kernel_tap % 3, height, breadth).reshape(
            samples, height * breadth, depth_in
        )
        per_sample = lax.dot_general(
            shifted, flat_up, (((1,), (1,)), ((0,), (0,))), preferred_element_type=jnp.float32
        )
        results.append(jnp.sum(per_sample.astype(jnp.bfloat16).astype(jnp.float32), axis=0))
    return jnp.stack(results, axis=0)


def adam_update(master, moment, second, gradient):
    moment_new = BETA_ONE * moment + (1.0 - BETA_ONE) * gradient
    second_new = BETA_TWO * second + (1.0 - BETA_TWO) * gradient * gradient
    step_size = moment_new / CORRECT_ONE / (jnp.sqrt(second_new / CORRECT_TWO) + ADAM_EPS)
    return (master - LEARN_RATE * step_size, moment_new, second_new)


def transpose_mesh(block):
    count = lax.axis_size("sample")
    pairs = [(row * count + col, col * count + row) for row in range(count) for col in range(count)]
    return lax.ppermute(block, ("sample", "filter"), pairs)


def exchange(payload, axis):
    return lax.all_to_all(payload, axis, 0, 0, tiled=True)


def tiled(block, axis):
    return jnp.tile(block, (lax.axis_size(axis), 1, 1, 1))


def summed(pieces):
    return jnp.sum(pieces.astype(jnp.float32), axis=0, keepdims=True)


def per_device(
    activations,
    cotangent,
    master_first,
    moment_first,
    second_first,
    master_second,
    moment_second,
    second_second,
):
    weight_first = master_first.astype(jnp.bfloat16)
    weight_second = master_second.astype(jnp.bfloat16)
    width = activations.shape[3]
    whole_input = exchange(tiled(transpose_mesh(activations), "filter"), "filter")
    partial_first = conv_forward(whole_input, weight_first).astype(jnp.bfloat16)
    joined = exchange(jnp.concatenate([tiled(cotangent, "sample"), partial_first], axis=3), "sample")
    whole_cotangent = joined[..., :width]
    pre_first = summed(joined[..., width:])
    hidden = group_silu(pre_first).astype(jnp.bfloat16)
    terms_second = adjoint_block(whole_cotangent, weight_second).astype(jnp.bfloat16)
    joined = exchange(
        jnp.concatenate([tiled(transpose_mesh(hidden), "filter"), terms_second], axis=3), "filter"
    )
    whole_hidden = joined[..., :width]
    hidden_grad = transpose_mesh(summed(joined[..., width:]))
    _, pullback = jax.vjp(group_silu, pre_first)
    pre_grad = pullback(hidden_grad)[0].astype(jnp.bfloat16)
    partial_second = conv_forward(whole_hidden, weight_second).astype(jnp.bfloat16)
    joined = exchange(jnp.concatenate([partial_second, tiled(pre_grad, "sample")], axis=3), "sample")
    pre_second = summed(joined[..., :width])
    whole_pre_grad = joined[..., width:]
    level_out = (activations.astype(jnp.float32) + pre_second).astype(jnp.bfloat16)
    terms_first = adjoint_block(whole_pre_grad, weight_first).astype(jnp.bfloat16)
    data_grad = transpose_mesh(summed(exchange(terms_first, "filter")))
    input_grad = (cotangent.astype(jnp.float32) + data_grad).astype(jnp.bfloat16)
    grad_second = tap_grad_sum(whole_hidden, whole_cotangent)
    grad_first = tap_grad_sum(whole_input, whole_pre_grad)
    new_master_first, new_moment_first, new_second_first = adam_update(
        master_first, moment_first, second_first, grad_first
    )
    new_master_second, new_moment_second, new_second_second = adam_update(
        master_second, moment_second, second_second, grad_second
    )
    return (
        level_out,
        input_grad,
        new_master_first,
        new_moment_first,
        new_second_first,
        new_master_second,
        new_moment_second,
        new_second_second,
    )


def solution(mesh):
    field = P("sample", None, None, "filter")
    taps = P(None, "sample", "filter")
    return jax.shard_map(
        per_device,
        mesh=mesh,
        in_specs=(field, field, taps, taps, taps, taps, taps, taps),
        out_specs=(field, field, taps, taps, taps, taps, taps, taps),
        check_vma=False,
    )
```

```python
import jax
import jax.numpy as jnp
from jax import lax
from jax.sharding import PartitionSpec as P

GROUP = 64

NORM_EPS = 1e-05
LEARN_RATE = 0.001
BETA_ONE = 0.9
BETA_TWO = 0.999
ADAM_EPS = 1e-08
CORRECT_ONE = 1.0 - 0.9**10
CORRECT_TWO = 1.0 - 0.999**10


def pad_slab(field):
    return jnp.pad(field, ((0, 0), (1, 1), (1, 1), (0, 0)))


def window(padded, row_start, column_start, height, breadth):
    return padded[:, row_start : row_start + height, column_start : column_start + breadth, :]


def conv_forward(source, weight):
    samples, height, breadth, depth_in = source.shape
    padded = pad_slab(source)
    summed = jnp.zeros((samples * height * breadth, weight.shape[2]), jnp.float32)
    for kernel_tap in range(9):
        shifted = window(padded, kernel_tap // 3, kernel_tap % 3, height, breadth)
        summed = summed + jnp.dot(
            shifted.reshape(samples * height * breadth, depth_in),
            weight[kernel_tap],
            preferred_element_type=jnp.float32,
        )
    return summed.reshape(samples, height, breadth, weight.shape[2])


def adjoint_block(upstream, weight):
    samples, height, breadth, depth_out = upstream.shape
    padded = pad_slab(upstream)
    summed = jnp.zeros((samples * height * breadth, weight.shape[1]), jnp.float32)
    for kernel_tap in range(9):
        shifted = window(padded, 2 - kernel_tap // 3, 2 - kernel_tap % 3, height, breadth)
        summed = summed + lax.dot_general(
            shifted.reshape(samples * height * breadth, depth_out),
            weight[kernel_tap],
            (((1,), (1,)), ((), ())),
            preferred_element_type=jnp.float32,
        )
    return summed.reshape(samples, height, breadth, weight.shape[1])


def group_silu(pre_act):
    samples, height, breadth, depth_all = pre_act.shape
    grouped = pre_act.reshape(samples, height, breadth, depth_all // GROUP, GROUP)
    center = jnp.mean(grouped, axis=(1, 2, 4), keepdims=True)
    deviation = grouped - center
    spread = jnp.mean(deviation * deviation, axis=(1, 2, 4), keepdims=True)
    return jax.nn.silu(deviation * lax.rsqrt(spread + NORM_EPS)).reshape(pre_act.shape)


def tap_grad_sum(source, upstream):
    samples, height, breadth, depth_in = source.shape
    padded = pad_slab(source)
    flat_up = upstream.reshape(samples, height * breadth, upstream.shape[3])
    results = []
    for kernel_tap in range(9):
        shifted = window(padded, kernel_tap // 3, kernel_tap % 3, height, breadth).reshape(
            samples, height * breadth, depth_in
        )
        per_sample = lax.dot_general(
            shifted, flat_up, (((1,), (1,)), ((0,), (0,))), preferred_element_type=jnp.float32
        )
        results.append(jnp.sum(per_sample.astype(jnp.bfloat16).astype(jnp.float32), axis=0))
    return jnp.stack(results, axis=0)


def adam_update(master, moment, second, gradient):
    moment_new = BETA_ONE * moment + (1.0 - BETA_ONE) * gradient
    second_new = BETA_TWO * second + (1.0 - BETA_TWO) * gradient * gradient
    step_size = moment_new / CORRECT_ONE / (jnp.sqrt(second_new / CORRECT_TWO) + ADAM_EPS)
    return (master - LEARN_RATE * step_size, moment_new, second_new)


def transpose_mesh(block):
    count = lax.axis_size("sample")
    pairs = [(row * count + col, col * count + row) for row in range(count) for col in range(count)]
    return lax.ppermute(block, ("sample", "filter"), pairs)


def exchange(payload, axis):
    return lax.all_to_all(payload, axis, 0, 0, tiled=True)


def tiled(block, axis):
    return jnp.tile(block, (lax.axis_size(axis), 1, 1, 1))


def summed(pieces):
    return jnp.sum(pieces.astype(jnp.float32), axis=0, keepdims=True)


def per_device(
    activations,
    cotangent,
    master_first,
    moment_first,
    second_first,
    master_second,
    moment_second,
    second_second,
):
    weight_first = master_first.astype(jnp.bfloat16)
    swapped_second = transpose_mesh(master_second.astype(jnp.bfloat16))
    width = activations.shape[3]
    joined = exchange(
        jnp.concatenate(
            [tiled(transpose_mesh(activations), "filter"), tiled(transpose_mesh(cotangent), "filter")],
            axis=3,
        ),
        "filter",
    )
    whole_input = joined[..., :width]
    whole_cotangent = joined[..., width:]
    partial_first = conv_forward(whole_input, weight_first).astype(jnp.bfloat16)
    terms_second = adjoint_block(whole_cotangent, swapped_second).astype(jnp.bfloat16)
    joined = exchange(jnp.concatenate([partial_first, terms_second], axis=3), "sample")
    pre_first = summed(joined[..., :width])
    hidden_grad = summed(joined[..., width:])
    hidden = group_silu(pre_first).astype(jnp.bfloat16)
    _, pullback = jax.vjp(group_silu, pre_first)
    pre_grad = pullback(hidden_grad)[0].astype(jnp.bfloat16)
    joined = exchange(
        jnp.concatenate([tiled(hidden, "sample"), tiled(pre_grad, "sample")], axis=3), "sample"
    )
    whole_hidden = joined[..., :width]
    whole_pre_grad = joined[..., width:]
    partial_second = conv_forward(whole_hidden, swapped_second).astype(jnp.bfloat16)
    terms_first = adjoint_block(whole_pre_grad, weight_first).astype(jnp.bfloat16)
    joined = transpose_mesh(
        summed(exchange(jnp.concatenate([partial_second, terms_first], axis=3), "filter"))
    )
    pre_second = joined[..., :width]
    data_grad = joined[..., width:]
    level_out = (activations.astype(jnp.float32) + pre_second).astype(jnp.bfloat16)
    input_grad = (cotangent.astype(jnp.float32) + data_grad).astype(jnp.bfloat16)
    grad_second = transpose_mesh(tap_grad_sum(whole_hidden, whole_cotangent))
    grad_first = tap_grad_sum(whole_input, whole_pre_grad)
    new_master_first, new_moment_first, new_second_first = adam_update(
        master_first, moment_first, second_first, grad_first
    )
    new_master_second, new_moment_second, new_second_second = adam_update(
        master_second, moment_second, second_second, grad_second
    )
    return (
        level_out,
        input_grad,
        new_master_first,
        new_moment_first,
        new_second_first,
        new_master_second,
        new_moment_second,
        new_second_second,
    )


def solution(mesh):
    field = P("sample", None, None, "filter")
    taps = P(None, "sample", "filter")
    return jax.shard_map(
        per_device,
        mesh=mesh,
        in_specs=(field, field, taps, taps, taps, taps, taps, taps),
        out_specs=(field, field, taps, taps, taps, taps, taps, taps),
        check_vma=False,
    )
```

```python
import jax
import jax.numpy as jnp
from jax import lax
from jax.sharding import PartitionSpec as P

GROUP = 64

NORM_EPS = 1e-05
LEARN_RATE = 0.001
BETA_ONE = 0.9
BETA_TWO = 0.999
ADAM_EPS = 1e-08
CORRECT_ONE = 1.0 - 0.9**10
CORRECT_TWO = 1.0 - 0.999**10


def pad_slab(field):
    return jnp.pad(field, ((0, 0), (1, 1), (1, 1), (0, 0)))


def window(padded, row_start, column_start, height, breadth):
    return padded[:, row_start : row_start + height, column_start : column_start + breadth, :]


def conv_forward(source, weight):
    taps = weight.reshape((3, 3) + weight.shape[1:])
    return lax.conv_general_dilated(
        source,
        taps,
        (1, 1),
        ((1, 1), (1, 1)),
        dimension_numbers=("NHWC", "HWIO", "NHWC"),
        preferred_element_type=jnp.float32,
    )


def adjoint_block(upstream, weight):
    taps = jnp.swapaxes(weight.reshape((3, 3) + weight.shape[1:])[::-1, ::-1], 2, 3)
    return lax.conv_general_dilated(
        upstream,
        taps,
        (1, 1),
        ((1, 1), (1, 1)),
        dimension_numbers=("NHWC", "HWIO", "NHWC"),
        preferred_element_type=jnp.float32,
    )


def group_silu(pre_act):
    samples, height, breadth, depth_all = pre_act.shape
    grouped = pre_act.reshape(samples, height, breadth, depth_all // GROUP, GROUP)
    center = jnp.mean(grouped, axis=(1, 2, 4), keepdims=True)
    deviation = grouped - center
    spread = jnp.mean(deviation * deviation, axis=(1, 2, 4), keepdims=True)
    return jax.nn.silu(deviation * lax.rsqrt(spread + NORM_EPS)).reshape(pre_act.shape)


def tap_grad_sum(source, upstream):
    samples, height, breadth, depth_in = source.shape
    padded = pad_slab(source)
    flat_up = upstream.reshape(samples, height * breadth, upstream.shape[3])
    results = []
    for kernel_tap in range(9):
        shifted = window(padded, kernel_tap // 3, kernel_tap % 3, height, breadth).reshape(
            samples, height * breadth, depth_in
        )
        per_sample = lax.dot_general(
            shifted, flat_up, (((1,), (1,)), ((0,), (0,))), preferred_element_type=jnp.float32
        )
        results.append(jnp.sum(per_sample.astype(jnp.bfloat16).astype(jnp.float32), axis=0))
    return jnp.stack(results, axis=0)


def adam_update(master, moment, second, gradient):
    moment_new = BETA_ONE * moment + (1.0 - BETA_ONE) * gradient
    second_new = BETA_TWO * second + (1.0 - BETA_TWO) * gradient * gradient
    step_size = moment_new / CORRECT_ONE / (jnp.sqrt(second_new / CORRECT_TWO) + ADAM_EPS)
    return (master - LEARN_RATE * step_size, moment_new, second_new)


def transpose_mesh(block):
    count = lax.axis_size("sample")
    pairs = [(row * count + col, col * count + row) for row in range(count) for col in range(count)]
    return lax.ppermute(block, ("sample", "filter"), pairs)


def exchange(payload, axis):
    return lax.all_to_all(payload, axis, 0, 0, tiled=True)


def tiled(block, axis):
    return jnp.tile(block, (lax.axis_size(axis), 1, 1, 1))


def summed(pieces):
    return jnp.sum(pieces.astype(jnp.float32), axis=0, keepdims=True)


def per_device(
    activations,
    cotangent,
    master_first,
    moment_first,
    second_first,
    master_second,
    moment_second,
    second_second,
):
    weight_first = master_first.astype(jnp.bfloat16)
    weight_second = master_second.astype(jnp.bfloat16)
    width = activations.shape[3]
    whole_input = exchange(tiled(transpose_mesh(activations), "filter"), "filter")
    partial_first = conv_forward(whole_input, weight_first).astype(jnp.bfloat16)
    joined = exchange(jnp.concatenate([tiled(cotangent, "sample"), partial_first], axis=3), "sample")
    whole_cotangent = joined[..., :width]
    pre_first = summed(joined[..., width:])
    hidden = group_silu(pre_first).astype(jnp.bfloat16)
    terms_second = adjoint_block(whole_cotangent, weight_second).astype(jnp.bfloat16)
    joined = exchange(
        jnp.concatenate([tiled(transpose_mesh(hidden), "filter"), terms_second], axis=3), "filter"
    )
    whole_hidden = joined[..., :width]
    hidden_grad = transpose_mesh(summed(joined[..., width:]))
    _, pullback = jax.vjp(group_silu, pre_first)
    pre_grad = pullback(hidden_grad)[0].astype(jnp.bfloat16)
    partial_second = conv_forward(whole_hidden, weight_second).astype(jnp.bfloat16)
    joined = exchange(jnp.concatenate([partial_second, tiled(pre_grad, "sample")], axis=3), "sample")
    pre_second = summed(joined[..., :width])
    whole_pre_grad = joined[..., width:]
    level_out = (activations.astype(jnp.float32) + pre_second).astype(jnp.bfloat16)
    terms_first = adjoint_block(whole_pre_grad, weight_first).astype(jnp.bfloat16)
    data_grad = transpose_mesh(summed(exchange(terms_first, "filter")))
    input_grad = (cotangent.astype(jnp.float32) + data_grad).astype(jnp.bfloat16)
    grad_second = tap_grad_sum(whole_hidden, whole_cotangent)
    grad_first = tap_grad_sum(whole_input, whole_pre_grad)
    new_master_first, new_moment_first, new_second_first = adam_update(
        master_first, moment_first, second_first, grad_first
    )
    new_master_second, new_moment_second, new_second_second = adam_update(
        master_second, moment_second, second_second, grad_second
    )
    return (
        level_out,
        input_grad,
        new_master_first,
        new_moment_first,
        new_second_first,
        new_master_second,
        new_moment_second,
        new_second_second,
    )


def solution(mesh):
    field = P("sample", None, None, "filter")
    taps = P(None, "sample", "filter")
    return jax.shard_map(
        per_device,
        mesh=mesh,
        in_specs=(field, field, taps, taps, taps, taps, taps, taps),
        out_specs=(field, field, taps, taps, taps, taps, taps, taps),
        check_vma=False,
    )
```

```python
import jax
import jax.numpy as jnp
from jax import lax
from jax.sharding import PartitionSpec as P

GROUP = 64

NORM_EPS = 1e-05
LEARN_RATE = 0.001
BETA_ONE = 0.9
BETA_TWO = 0.999
ADAM_EPS = 1e-08
CORRECT_ONE = 1.0 - 0.9**10
CORRECT_TWO = 1.0 - 0.999**10


def pad_slab(field):
    return jnp.pad(field, ((0, 0), (1, 1), (1, 1), (0, 0)))


def window(padded, row_start, column_start, height, breadth):
    return padded[:, row_start : row_start + height, column_start : column_start + breadth, :]


def conv_forward(source, weight):
    taps = weight.reshape((3, 3) + weight.shape[1:])
    return lax.conv_general_dilated(
        source,
        taps,
        (1, 1),
        ((1, 1), (1, 1)),
        dimension_numbers=("NHWC", "HWIO", "NHWC"),
        preferred_element_type=jnp.float32,
    )


def adjoint_block(upstream, weight):
    taps = jnp.swapaxes(weight.reshape((3, 3) + weight.shape[1:])[::-1, ::-1], 2, 3)
    return lax.conv_general_dilated(
        upstream,
        taps,
        (1, 1),
        ((1, 1), (1, 1)),
        dimension_numbers=("NHWC", "HWIO", "NHWC"),
        preferred_element_type=jnp.float32,
    )


def group_silu(pre_act):
    samples, height, breadth, depth_all = pre_act.shape
    grouped = pre_act.reshape(samples, height, breadth, depth_all // GROUP, GROUP)
    center = jnp.mean(grouped, axis=(1, 2, 4), keepdims=True)
    deviation = grouped - center
    spread = jnp.mean(deviation * deviation, axis=(1, 2, 4), keepdims=True)
    return jax.nn.silu(deviation * lax.rsqrt(spread + NORM_EPS)).reshape(pre_act.shape)


def tap_grad_sum(source, upstream):
    samples, height, breadth, depth_in = source.shape
    padded = pad_slab(source)
    flat_up = upstream.reshape(samples, height * breadth, upstream.shape[3])
    results = []
    for kernel_tap in range(9):
        shifted = window(padded, kernel_tap // 3, kernel_tap % 3, height, breadth).reshape(
            samples, height * breadth, depth_in
        )
        per_sample = lax.dot_general(
            shifted, flat_up, (((1,), (1,)), ((0,), (0,))), preferred_element_type=jnp.float32
        )
        results.append(jnp.sum(per_sample.astype(jnp.bfloat16).astype(jnp.float32), axis=0))
    return jnp.stack(results, axis=0)


def adam_update(master, moment, second, gradient):
    moment_new = BETA_ONE * moment + (1.0 - BETA_ONE) * gradient
    second_new = BETA_TWO * second + (1.0 - BETA_TWO) * gradient * gradient
    step_size = moment_new / CORRECT_ONE / (jnp.sqrt(second_new / CORRECT_TWO) + ADAM_EPS)
    return (master - LEARN_RATE * step_size, moment_new, second_new)


def transpose_mesh(block):
    count = lax.axis_size("sample")
    pairs = [(row * count + col, col * count + row) for row in range(count) for col in range(count)]
    return lax.ppermute(block, ("sample", "filter"), pairs)


def exchange(payload, axis):
    return lax.all_to_all(payload, axis, 0, 0, tiled=True)


def tiled(block, axis):
    return jnp.tile(block, (lax.axis_size(axis), 1, 1, 1))


def summed(pieces):
    return jnp.sum(pieces.astype(jnp.float32), axis=0, keepdims=True)


def per_device(
    activations,
    cotangent,
    master_first,
    moment_first,
    second_first,
    master_second,
    moment_second,
    second_second,
):
    weight_first = master_first.astype(jnp.bfloat16)
    weight_second = master_second.astype(jnp.bfloat16)
    width = activations.shape[3]
    whole_input = exchange(tiled(transpose_mesh(activations), "filter"), "filter")
    partial_first = conv_forward(whole_input, weight_first).astype(jnp.bfloat16)
    joined = exchange(jnp.concatenate([tiled(cotangent, "sample"), partial_first], axis=3), "sample")
    whole_cotangent = joined[..., :width]
    pre_first = summed(joined[..., width:])
    hidden = group_silu(pre_first).astype(jnp.bfloat16)
    terms_second = adjoint_block(whole_cotangent, weight_second).astype(jnp.bfloat16)
    joined = exchange(
        jnp.concatenate([tiled(transpose_mesh(hidden), "filter"), terms_second], axis=3), "filter"
    )
    whole_hidden = joined[..., :width]
    hidden_grad = transpose_mesh(summed(joined[..., width:]))
    _, pullback = jax.vjp(group_silu, pre_first)
    pre_grad = pullback(hidden_grad)[0].astype(jnp.bfloat16)
    partial_second = conv_forward(whole_hidden, weight_second).astype(jnp.bfloat16)
    joined = exchange(jnp.concatenate([partial_second, tiled(pre_grad, "sample")], axis=3), "sample")
    pre_second = summed(joined[..., :width])
    whole_pre_grad = joined[..., width:]
    level_out = (activations.astype(jnp.float32) + pre_second).astype(jnp.bfloat16)
    terms_first = adjoint_block(whole_pre_grad, weight_first).astype(jnp.bfloat16)
    data_grad = transpose_mesh(summed(exchange(terms_first, "filter")))
    input_grad = (cotangent.astype(jnp.float32) + data_grad).astype(jnp.bfloat16)
    deferred_hidden, deferred_cotangent, _ = lax.optimization_barrier((whole_hidden, whole_cotangent, joined))
    grad_second = tap_grad_sum(deferred_hidden, deferred_cotangent)
    grad_first = tap_grad_sum(whole_input, whole_pre_grad)
    new_master_first, new_moment_first, new_second_first = adam_update(
        master_first, moment_first, second_first, grad_first
    )
    new_master_second, new_moment_second, new_second_second = adam_update(
        master_second, moment_second, second_second, grad_second
    )
    return (
        level_out,
        input_grad,
        new_master_first,
        new_moment_first,
        new_second_first,
        new_master_second,
        new_moment_second,
        new_second_second,
    )


def solution(mesh):
    field = P("sample", None, None, "filter")
    taps = P(None, "sample", "filter")
    return jax.shard_map(
        per_device,
        mesh=mesh,
        in_specs=(field, field, taps, taps, taps, taps, taps, taps),
        out_specs=(field, field, taps, taps, taps, taps, taps, taps),
        check_vma=False,
    )
```

```python
import jax
import jax.numpy as jnp
from jax import lax
from jax.sharding import PartitionSpec as P

GROUP = 64

NORM_EPS = 1e-05
LEARN_RATE = 0.001
BETA_ONE = 0.9
BETA_TWO = 0.999
ADAM_EPS = 1e-08
CORRECT_ONE = 1.0 - 0.9**10
CORRECT_TWO = 1.0 - 0.999**10


def pad_slab(field):
    return jnp.pad(field, ((0, 0), (1, 1), (1, 1), (0, 0)))


def window(padded, row_start, column_start, height, breadth):
    return padded[:, row_start : row_start + height, column_start : column_start + breadth, :]


def conv_forward(source, weight):
    taps = weight.reshape((3, 3) + weight.shape[1:])
    return lax.conv_general_dilated(
        source,
        taps,
        (1, 1),
        ((1, 1), (1, 1)),
        dimension_numbers=("NHWC", "HWIO", "NHWC"),
        preferred_element_type=jnp.float32,
    )


def adjoint_block(upstream, weight):
    taps = jnp.swapaxes(weight.reshape((3, 3) + weight.shape[1:])[::-1, ::-1], 2, 3)
    return lax.conv_general_dilated(
        upstream,
        taps,
        (1, 1),
        ((1, 1), (1, 1)),
        dimension_numbers=("NHWC", "HWIO", "NHWC"),
        preferred_element_type=jnp.float32,
    )


def group_silu(pre_act):
    samples, height, breadth, depth_all = pre_act.shape
    grouped = pre_act.reshape(samples, height, breadth, depth_all // GROUP, GROUP)
    center = jnp.mean(grouped, axis=(1, 2, 4), keepdims=True)
    deviation = grouped - center
    spread = jnp.mean(deviation * deviation, axis=(1, 2, 4), keepdims=True)
    return jax.nn.silu(deviation * lax.rsqrt(spread + NORM_EPS)).reshape(pre_act.shape)


def tap_grad_sum(source, upstream):
    samples, height, breadth, depth_in = source.shape
    padded = pad_slab(source)
    flat_up = upstream.reshape(samples, height * breadth, upstream.shape[3])
    results = []
    for kernel_tap in range(9):
        shifted = window(padded, kernel_tap // 3, kernel_tap % 3, height, breadth).reshape(
            samples, height * breadth, depth_in
        )
        per_sample = lax.dot_general(
            shifted, flat_up, (((1,), (1,)), ((0,), (0,))), preferred_element_type=jnp.float32
        )
        results.append(jnp.sum(per_sample.astype(jnp.bfloat16).astype(jnp.float32), axis=0))
    return jnp.stack(results, axis=0)


def adam_update(master, moment, second, gradient):
    moment_new = BETA_ONE * moment + (1.0 - BETA_ONE) * gradient
    second_new = BETA_TWO * second + (1.0 - BETA_TWO) * gradient * gradient
    step_size = moment_new / CORRECT_ONE / (jnp.sqrt(second_new / CORRECT_TWO) + ADAM_EPS)
    return (master - LEARN_RATE * step_size, moment_new, second_new)


def transpose_mesh(block):
    count = lax.axis_size("sample")
    pairs = [(row * count + col, col * count + row) for row in range(count) for col in range(count)]
    return lax.ppermute(block, ("sample", "filter"), pairs)


def exchange(payload, axis):
    return lax.all_to_all(payload, axis, 0, 0, tiled=True)


def tiled(block, axis):
    return jnp.tile(block, (lax.axis_size(axis), 1, 1, 1))


def summed(pieces):
    return jnp.sum(pieces.astype(jnp.float32), axis=0, keepdims=True)


def per_device(
    activations,
    cotangent,
    master_first,
    moment_first,
    second_first,
    master_second,
    moment_second,
    second_second,
):
    weight_first = master_first.astype(jnp.bfloat16)
    weight_second = master_second.astype(jnp.bfloat16)
    width = activations.shape[3]
    whole_input = exchange(tiled(transpose_mesh(activations), "filter"), "filter")
    partial_first = conv_forward(whole_input, weight_first).astype(jnp.bfloat16)
    joined = exchange(jnp.concatenate([tiled(cotangent, "sample"), partial_first], axis=3), "sample")
    whole_cotangent = joined[..., :width]
    pre_first = summed(joined[..., width:])
    hidden = group_silu(pre_first).astype(jnp.bfloat16)
    terms_second = adjoint_block(whole_cotangent, weight_second).astype(jnp.bfloat16)
    joined = exchange(
        jnp.concatenate([tiled(transpose_mesh(hidden), "filter"), terms_second], axis=3), "filter"
    )
    whole_hidden = joined[..., :width]
    hidden_grad = transpose_mesh(summed(joined[..., width:]))
    _, pullback = jax.vjp(group_silu, pre_first)
    pre_grad = pullback(hidden_grad)[0].astype(jnp.bfloat16)
    partial_second = conv_forward(whole_hidden, weight_second).astype(jnp.bfloat16)
    payload = jnp.concatenate([partial_second, tiled(pre_grad, "sample")], axis=3)
    joined = exchange(payload, "sample")
    pre_second = summed(joined[..., :width])
    whole_pre_grad = joined[..., width:]
    level_out = (activations.astype(jnp.float32) + pre_second).astype(jnp.bfloat16)
    terms_first = adjoint_block(whole_pre_grad, weight_first).astype(jnp.bfloat16)
    data_grad = transpose_mesh(summed(exchange(terms_first, "filter")))
    input_grad = (cotangent.astype(jnp.float32) + data_grad).astype(jnp.bfloat16)
    deferred_hidden, deferred_cotangent, _ = lax.optimization_barrier((whole_hidden, whole_cotangent, payload))
    grad_second = tap_grad_sum(deferred_hidden, deferred_cotangent)
    grad_first = tap_grad_sum(whole_input, whole_pre_grad)
    new_master_first, new_moment_first, new_second_first = adam_update(
        master_first, moment_first, second_first, grad_first
    )
    new_master_second, new_moment_second, new_second_second = adam_update(
        master_second, moment_second, second_second, grad_second
    )
    return (
        level_out,
        input_grad,
        new_master_first,
        new_moment_first,
        new_second_first,
        new_master_second,
        new_moment_second,
        new_second_second,
    )


def solution(mesh):
    field = P("sample", None, None, "filter")
    taps = P(None, "sample", "filter")
    return jax.shard_map(
        per_device,
        mesh=mesh,
        in_specs=(field, field, taps, taps, taps, taps, taps, taps),
        out_specs=(field, field, taps, taps, taps, taps, taps, taps),
        check_vma=False,
    )
```

```python
import jax
import jax.numpy as jnp
from jax import lax
from jax.experimental.layout import Layout, with_layout_constraint
from jax.sharding import PartitionSpec as P

GROUP = 64

NORM_EPS = 1e-05
LEARN_RATE = 0.001
BETA_ONE = 0.9
BETA_TWO = 0.999
ADAM_EPS = 1e-08
CORRECT_ONE = 1.0 - 0.9**10
CORRECT_TWO = 1.0 - 0.999**10


def pad_slab(field):
    return jnp.pad(field, ((0, 0), (1, 1), (1, 1), (0, 0)))


def window(padded, row_start, column_start, height, breadth):
    return padded[:, row_start : row_start + height, column_start : column_start + breadth, :]


def conv_forward(source, weight):
    taps = weight.reshape((3, 3) + weight.shape[1:])
    return lax.conv_general_dilated(
        source,
        taps,
        (1, 1),
        ((1, 1), (1, 1)),
        dimension_numbers=("NHWC", "HWIO", "NHWC"),
        preferred_element_type=jnp.float32,
    )


def adjoint_block(upstream, weight):
    taps = jnp.swapaxes(weight.reshape((3, 3) + weight.shape[1:])[::-1, ::-1], 2, 3)
    return lax.conv_general_dilated(
        upstream,
        taps,
        (1, 1),
        ((1, 1), (1, 1)),
        dimension_numbers=("NHWC", "HWIO", "NHWC"),
        preferred_element_type=jnp.float32,
    )


def group_silu(pre_act):
    samples, height, breadth, depth_all = pre_act.shape
    grouped = pre_act.reshape(samples, height, breadth, depth_all // GROUP, GROUP)
    center = jnp.mean(grouped, axis=(1, 2, 4), keepdims=True)
    deviation = grouped - center
    spread = jnp.mean(deviation * deviation, axis=(1, 2, 4), keepdims=True)
    return jax.nn.silu(deviation * lax.rsqrt(spread + NORM_EPS)).reshape(pre_act.shape)


def tap_grad_sum(source, upstream):
    samples, height, breadth, depth_in = source.shape
    padded = pad_slab(source)
    flat_up = upstream.reshape(samples, height * breadth, upstream.shape[3])
    results = []
    for kernel_tap in range(9):
        shifted = window(padded, kernel_tap // 3, kernel_tap % 3, height, breadth).reshape(
            samples, height * breadth, depth_in
        )
        per_sample = lax.dot_general(
            shifted, flat_up, (((1,), (1,)), ((0,), (0,))), preferred_element_type=jnp.float32
        )
        results.append(jnp.sum(per_sample.astype(jnp.bfloat16).astype(jnp.float32), axis=0))
    return jnp.stack(results, axis=0)


def adam_update(master, moment, second, gradient):
    moment_new = BETA_ONE * moment + (1.0 - BETA_ONE) * gradient
    second_new = BETA_TWO * second + (1.0 - BETA_TWO) * gradient * gradient
    step_size = moment_new / CORRECT_ONE / (jnp.sqrt(second_new / CORRECT_TWO) + ADAM_EPS)
    return (master - LEARN_RATE * step_size, moment_new, second_new)


def transpose_mesh(block):
    count = lax.axis_size("sample")
    pairs = [(row * count + col, col * count + row) for row in range(count) for col in range(count)]
    return lax.ppermute(block, ("sample", "filter"), pairs)


def exchange(payload, axis):
    return lax.all_to_all(payload, axis, 0, 0, tiled=True)


def sample_major(field):
    return with_layout_constraint(field, Layout(major_to_minor=(0, 1, 2, 3)))


def tiled(block, axis):
    return jnp.tile(block, (lax.axis_size(axis), 1, 1, 1))


def summed(pieces):
    return jnp.sum(pieces.astype(jnp.float32), axis=0, keepdims=True)


def per_device(
    activations,
    cotangent,
    master_first,
    moment_first,
    second_first,
    master_second,
    moment_second,
    second_second,
):
    weight_first = master_first.astype(jnp.bfloat16)
    weight_second = master_second.astype(jnp.bfloat16)
    width = activations.shape[3]
    whole_input = exchange(tiled(transpose_mesh(activations), "filter"), "filter")
    partial_first = sample_major(conv_forward(whole_input, weight_first).astype(jnp.bfloat16))
    joined = exchange(jnp.concatenate([tiled(cotangent, "sample"), partial_first], axis=3), "sample")
    whole_cotangent = joined[..., :width]
    pre_first = summed(joined[..., width:])
    hidden = group_silu(pre_first).astype(jnp.bfloat16)
    terms_second = sample_major(adjoint_block(whole_cotangent, weight_second).astype(jnp.bfloat16))
    joined = exchange(
        jnp.concatenate([tiled(transpose_mesh(hidden), "filter"), terms_second], axis=3), "filter"
    )
    whole_hidden = joined[..., :width]
    hidden_grad = transpose_mesh(summed(joined[..., width:]))
    _, pullback = jax.vjp(group_silu, pre_first)
    pre_grad = pullback(hidden_grad)[0].astype(jnp.bfloat16)
    partial_second = sample_major(conv_forward(whole_hidden, weight_second).astype(jnp.bfloat16))
    joined = exchange(jnp.concatenate([partial_second, tiled(pre_grad, "sample")], axis=3), "sample")
    pre_second = summed(joined[..., :width])
    whole_pre_grad = joined[..., width:]
    level_out = (activations.astype(jnp.float32) + pre_second).astype(jnp.bfloat16)
    terms_first = sample_major(adjoint_block(whole_pre_grad, weight_first).astype(jnp.bfloat16))
    data_grad = transpose_mesh(summed(exchange(terms_first, "filter")))
    input_grad = (cotangent.astype(jnp.float32) + data_grad).astype(jnp.bfloat16)
    deferred_hidden, deferred_cotangent, _ = lax.optimization_barrier((whole_hidden, whole_cotangent, joined))
    grad_second = tap_grad_sum(deferred_hidden, deferred_cotangent)
    grad_first = tap_grad_sum(whole_input, whole_pre_grad)
    new_master_first, new_moment_first, new_second_first = adam_update(
        master_first, moment_first, second_first, grad_first
    )
    new_master_second, new_moment_second, new_second_second = adam_update(
        master_second, moment_second, second_second, grad_second
    )
    return (
        level_out,
        input_grad,
        new_master_first,
        new_moment_first,
        new_second_first,
        new_master_second,
        new_moment_second,
        new_second_second,
    )


def solution(mesh):
    field = P("sample", None, None, "filter")
    taps = P(None, "sample", "filter")
    return jax.shard_map(
        per_device,
        mesh=mesh,
        in_specs=(field, field, taps, taps, taps, taps, taps, taps),
        out_specs=(field, field, taps, taps, taps, taps, taps, taps),
        check_vma=False,
    )
```

```python
import jax
import jax.numpy as jnp
from jax import lax
from jax.experimental.layout import Layout, with_layout_constraint
from jax.sharding import PartitionSpec as P

GROUP = 64

NORM_EPS = 1e-05
LEARN_RATE = 0.001
BETA_ONE = 0.9
BETA_TWO = 0.999
ADAM_EPS = 1e-08
CORRECT_ONE = 1.0 - 0.9**10
CORRECT_TWO = 1.0 - 0.999**10


def pad_slab(field):
    return jnp.pad(field, ((0, 0), (1, 1), (1, 1), (0, 0)))


def window(padded, row_start, column_start, height, breadth):
    return padded[:, row_start : row_start + height, column_start : column_start + breadth, :]


def conv_forward(source, weight):
    taps = weight.reshape((3, 3) + weight.shape[1:])
    return lax.conv_general_dilated(
        source,
        taps,
        (1, 1),
        ((1, 1), (1, 1)),
        dimension_numbers=("NHWC", "HWIO", "NHWC"),
        preferred_element_type=jnp.float32,
    )


def adjoint_block(upstream, weight):
    taps = jnp.swapaxes(weight.reshape((3, 3) + weight.shape[1:])[::-1, ::-1], 2, 3)
    return lax.conv_general_dilated(
        upstream,
        taps,
        (1, 1),
        ((1, 1), (1, 1)),
        dimension_numbers=("NHWC", "HWIO", "NHWC"),
        preferred_element_type=jnp.float32,
    )


def group_silu(pre_act):
    samples, height, breadth, depth_all = pre_act.shape
    grouped = pre_act.reshape(samples, height, breadth, depth_all // GROUP, GROUP)
    center = jnp.mean(grouped, axis=(1, 2, 4), keepdims=True)
    deviation = grouped - center
    spread = jnp.mean(deviation * deviation, axis=(1, 2, 4), keepdims=True)
    return jax.nn.silu(deviation * lax.rsqrt(spread + NORM_EPS)).reshape(pre_act.shape)


def tap_grad_sum(source, upstream):
    samples, height, breadth, depth_in = source.shape
    padded = pad_slab(source)
    flat_up = upstream.reshape(samples, height * breadth, upstream.shape[3])
    results = []
    for kernel_tap in range(9):
        shifted = window(padded, kernel_tap // 3, kernel_tap % 3, height, breadth).reshape(
            samples, height * breadth, depth_in
        )
        per_sample = lax.dot_general(
            shifted, flat_up, (((1,), (1,)), ((0,), (0,))), preferred_element_type=jnp.float32
        )
        results.append(jnp.sum(per_sample.astype(jnp.bfloat16).astype(jnp.float32), axis=0))
    return jnp.stack(results, axis=0)


def adam_update(master, moment, second, gradient):
    moment_new = BETA_ONE * moment + (1.0 - BETA_ONE) * gradient
    second_new = BETA_TWO * second + (1.0 - BETA_TWO) * gradient * gradient
    step_size = moment_new / CORRECT_ONE / (jnp.sqrt(second_new / CORRECT_TWO) + ADAM_EPS)
    return (master - LEARN_RATE * step_size, moment_new, second_new)


def transpose_mesh(block):
    count = lax.axis_size("sample")
    pairs = [(row * count + col, col * count + row) for row in range(count) for col in range(count)]
    return lax.ppermute(block, ("sample", "filter"), pairs)


def exchange(payload, axis):
    return lax.all_to_all(payload, axis, 0, 0, tiled=True)


def sample_major(field):
    return with_layout_constraint(field, Layout(major_to_minor=(0, 1, 2, 3)))


def tiled(block, axis):
    return jnp.tile(block, (lax.axis_size(axis), 1, 1, 1))


def summed(pieces):
    return jnp.sum(pieces.astype(jnp.float32), axis=0, keepdims=True)


def per_device(
    activations,
    cotangent,
    master_first,
    moment_first,
    second_first,
    master_second,
    moment_second,
    second_second,
):
    weight_first = master_first.astype(jnp.bfloat16)
    weight_second = master_second.astype(jnp.bfloat16)
    width = activations.shape[3]
    whole_input = exchange(tiled(transpose_mesh(activations), "filter"), "filter")
    partial_first = sample_major(conv_forward(whole_input, weight_first).astype(jnp.bfloat16))
    joined = exchange(jnp.concatenate([tiled(cotangent, "sample"), partial_first], axis=3), "sample")
    whole_cotangent = joined[..., :width]
    pre_first = summed(joined[..., width:])
    hidden = group_silu(pre_first).astype(jnp.bfloat16)
    terms_second = sample_major(adjoint_block(whole_cotangent, weight_second).astype(jnp.bfloat16))
    joined = exchange(
        jnp.concatenate([tiled(transpose_mesh(hidden), "filter"), terms_second], axis=3), "filter"
    )
    whole_hidden = joined[..., :width]
    hidden_grad = transpose_mesh(summed(joined[..., width:]))
    _, pullback = jax.vjp(group_silu, pre_first)
    pre_grad = pullback(hidden_grad)[0].astype(jnp.bfloat16)
    partial_second = sample_major(conv_forward(whole_hidden, weight_second).astype(jnp.bfloat16))
    payload = jnp.concatenate([partial_second, tiled(pre_grad, "sample")], axis=3)
    joined = exchange(payload, "sample")
    pre_second = summed(joined[..., :width])
    whole_pre_grad = joined[..., width:]
    level_out = (activations.astype(jnp.float32) + pre_second).astype(jnp.bfloat16)
    terms_first = sample_major(adjoint_block(whole_pre_grad, weight_first).astype(jnp.bfloat16))
    data_grad = transpose_mesh(summed(exchange(terms_first, "filter")))
    input_grad = (cotangent.astype(jnp.float32) + data_grad).astype(jnp.bfloat16)
    deferred_hidden, deferred_cotangent, _ = lax.optimization_barrier((whole_hidden, whole_cotangent, payload))
    grad_second = tap_grad_sum(deferred_hidden, deferred_cotangent)
    grad_first = tap_grad_sum(whole_input, whole_pre_grad)
    new_master_first, new_moment_first, new_second_first = adam_update(
        master_first, moment_first, second_first, grad_first
    )
    new_master_second, new_moment_second, new_second_second = adam_update(
        master_second, moment_second, second_second, grad_second
    )
    return (
        level_out,
        input_grad,
        new_master_first,
        new_moment_first,
        new_second_first,
        new_master_second,
        new_moment_second,
        new_second_second,
    )


def solution(mesh):
    field = P("sample", None, None, "filter")
    taps = P(None, "sample", "filter")
    return jax.shard_map(
        per_device,
        mesh=mesh,
        in_specs=(field, field, taps, taps, taps, taps, taps, taps),
        out_specs=(field, field, taps, taps, taps, taps, taps, taps),
        check_vma=False,
    )
```
